1024 devices in a mesh: col: 32 (over y, x), af: 32 (over z, core).
Axes of the slice: x: 4, y: 8, z: 16, core: 2. Of those that a mesh axis runs over, the one named last changes fastest.
Arguments:
- inputs: bfloat16 [2, 64, 64, 8, 256], P(None, 'col', 'af'), may hold values from -6 to 6
- first_filters: bfloat16 [3, 3, 3, 256, 256], P(None, None, None, 'af'), may hold values from -0.125 to 0.125
- second_filters: bfloat16 [3, 3, 3, 256, 256], P(None, None, None, 'af'), may hold values from -0.1875 to 0.1875
Outputs:
- features: bfloat16 [2, 32, 32, 4, 256], P(None, 'col', None, None, 'af')
The draws below stay inside these ranges and needn't reach their ends.
All inputs are finite; a program needn't handle non-finite values.
Results may differ from the reference program's by a relative error of at most 0.011.
Values may be sent and summed in bfloat16 or wider, within the bound.
No kernel may reach another device: no remote copies, remote signals or barrier semaphores. Data moves between devices by JAX's collectives and lax.ppermute only.
A program may use at most 32 MiB of HBM per device.

```python
import jax
import jax.numpy as jnp
from jax import lax

C = 256
SAMPLES = 2
DEPTH = 64
HGT = 64
WID = 8


def raised(entries, key, source, target, shards_of, factor):
    def block_of(axis_at):
        return (jnp.arange(entries.shape[axis_at]) // (entries.shape[axis_at] // shards_of)).reshape((-1,) + (1,) * (entries.ndim - 1 - axis_at))

    first = jax.random.permutation(key, shards_of)[block_of(target)]
    second = (block_of(target) + shards_of // 2) % shards_of
    return jnp.where((block_of(source) == first) | (block_of(source) == second), factor * entries, entries)


def block_scale(stream_key, extent, cuts, smallest, largest):
    loudness = 1.0
    for axis_at, blocks in cuts:
        draws = jax.random.uniform(jax.random.fold_in(jax.random.fold_in(stream_key, 6), axis_at), (blocks,), jnp.float32, smallest / len(cuts), largest / len(cuts))
        loudness = loudness * jnp.repeat(jnp.exp(draws), extent[axis_at] // blocks).reshape((-1,) + (1,) * (len(extent) - 1 - axis_at))
    return loudness


def normal_values(own_key, extent, scale, limit, cuts=(), kind=jnp.bfloat16):
    factor_of = block_scale(own_key, extent, cuts, -0.22, 0.18) if cuts else 1.0
    values = jax.random.normal(own_key, extent, jnp.float32) * scale * factor_of
    return jnp.minimum(jnp.maximum(values, -limit), limit).astype(kind)


def heavy_noise(rng, shape, spread, most, split, heavy, dtype=jnp.bfloat16):
    drawn = spread * jax.random.normal(rng, shape, jnp.float32)
    if split:
        drawn = drawn * block_scale(rng, shape, split, -0.22, 0.18)
    return jnp.clip(raised(drawn, jax.random.fold_in(rng, 3), *heavy), -most, most).astype(dtype)


def setup_inputs(seed: int = 0) -> dict:
    arg_keys = jax.random.split(jax.random.key(seed), 4)
    return {
        "inputs": normal_values(arg_keys[0], (SAMPLES, DEPTH, HGT, WID, C), 1.0, 6.0, ((1, 32), (2, 32))),
        "first_filters": heavy_noise(arg_keys[1], (3, 3, 3, C, C), (27 * C) ** -0.5, 0.125, ((3, 32),), (3, 4, 32, 2.75)),
        "second_filters": heavy_noise(arg_keys[2], (3, 3, 3, C, C), (27 * C // 2) ** -0.5, 0.1875, ((3, 32),), (3, 4, 32, 2.75)),
    }


def convolve(volume, kernel, stride):
    return lax.conv_general_dilated(volume, kernel, (stride, stride, stride), ((1, 1), (1, 1), (1, 1)), dimension_numbers=("NDHWC", "DHWIO", "NDHWC"), preferred_element_type=jnp.float32)


def reference(inputs, first_filters, second_filters):
    hidden = jnp.maximum(convolve(inputs, first_filters, 1), 0.0).astype(jnp.bfloat16)
    return jnp.maximum(convolve(hidden, second_filters, 2), 0.0).astype(jnp.bfloat16)
```

```python
import jax
import jax.numpy as jnp
from jax import lax
from jax.sharding import PartitionSpec as P


def extended(block, sides, width):
    for axis, dim in sides:
        count = lax.axis_size(axis)
        forward = [(i, i + 1) for i in range(count - 1)]
        backward = [(target, source) for source, target in forward]
        low = lax.ppermute(
            lax.slice_in_dim(block, block.shape[dim] - width, None, axis=dim), axis, forward
        )
        high = lax.ppermute(lax.slice_in_dim(block, 0, width, axis=dim), axis, backward)
        block = jnp.concatenate([low, block, high], axis=dim)
    return block


def passed_along(array, axis, by):
    peers = lax.axis_size(axis)
    pairs = [(i, i + by) for i in range(peers) if 0 <= i + by < peers]
    return lax.ppermute(array, axis, pairs)


def convolve(volume, kernel, stride, row_pad, out_spec="NDHWC"):
    return lax.conv_general_dilated(
        volume,
        kernel,
        (stride, stride, stride),
        ((0, 0), (row_pad, row_pad), (1, 1)),
        dimension_numbers=("NDHWC", "DHWIO", out_spec),
        preferred_element_type=jnp.float32,
    )


def per_device(inputs, first_filters, second_filters):
    padded = extended(inputs, (("col", 1),), 1)
    gathered = lax.all_gather(padded, "af", axis=2, tiled=True)
    own_first = lax.all_to_all(first_filters, "af", split_axis=4, concat_axis=3, tiled=True)
    hidden = jnp.maximum(convolve(gathered, own_first, 1, 1), 0.0).astype(jnp.bfloat16)
    lower_plane = passed_along(hidden[:, -1:], "col", 1)
    stacked = jnp.concatenate([lower_plane, hidden], axis=1)
    partial = convolve(stacked, second_filters, 2, 1, out_spec="CNDHW")
    totals = lax.psum_scatter(partial, "af", scatter_dimension=0, tiled=True)
    return jnp.maximum(jnp.transpose(totals, (1, 2, 3, 4, 0)), 0.0).astype(jnp.bfloat16)


def solution(mesh):
    placed = (
        P(None, "col", "af", None, None),
        P(None, None, None, "af", None),
        P(None, None, None, "af", None),
    )
    return jax.shard_map(
        per_device,
        mesh=mesh,
        in_specs=placed,
        out_specs=P(None, "col", None, None, "af"),
        check_vma=False,
    )
```

```python
import jax
import jax.numpy as jnp
from jax import lax
from jax.sharding import PartitionSpec as P


def extended(block, sides, width):
    for axis, dim in sides:
        count = lax.axis_size(axis)
        forward = [(i, i + 1) for i in range(count - 1)]
        backward = [(target, source) for source, target in forward]
        low = lax.ppermute(
            lax.slice_in_dim(block, block.shape[dim] - width, None, axis=dim), axis, forward
        )
        high = lax.ppermute(lax.slice_in_dim(block, 0, width, axis=dim), axis, backward)
        block = jnp.concatenate([low, block, high], axis=dim)
    return block


def passed_along(array, axis, by):
    peers = lax.axis_size(axis)
    pairs = [(i, i + by) for i in range(peers) if 0 <= i + by < peers]
    return lax.ppermute(array, axis, pairs)


def convolve(volume, kernel, stride, row_pad, out_spec="NDHWC"):
    return lax.conv_general_dilated(
        volume,
        kernel,
        (stride, stride, stride),
        ((0, 0), (row_pad, row_pad), (1, 1)),
        dimension_numbers=("NDHWC", "DHWIO", out_spec),
        preferred_element_type=jnp.float32,
    )


def reduce_scattered(partial, axis):
    peers = lax.axis_size(axis)
    me = lax.axis_index(axis)
    levels = peers.bit_length() - 1
    blocks = partial.reshape((2,) * levels + (partial.shape[0] // peers,) + partial.shape[1:])
    for bit in range(levels):
        at = levels - 1 - bit
        mine = (me // (1 << bit)) % 2
        keep = lax.dynamic_index_in_dim(blocks, mine, axis=at, keepdims=False)
        give = lax.dynamic_index_in_dim(blocks, 1 - mine, axis=at, keepdims=False)
        pairs = [(i, i ^ (1 << bit)) for i in range(peers)]
        blocks = keep + lax.ppermute(give, axis, pairs)
    return blocks


def per_device(inputs, first_filters, second_filters):
    padded = extended(inputs, (("col", 1),), 1)
    gathered = lax.all_gather(padded, "af", axis=2, tiled=True)
    own_first = lax.all_to_all(first_filters, "af", split_axis=4, concat_axis=3, tiled=True)
    hidden = jnp.maximum(convolve(gathered, own_first, 1, 1), 0.0).astype(jnp.bfloat16)
    lower_plane = passed_along(hidden[:, -1:], "col", 1)
    stacked = jnp.concatenate([lower_plane, hidden], axis=1)
    partial = convolve(stacked, second_filters, 2, 1, out_spec="CNDHW")
    totals = reduce_scattered(partial, "af")
    return jnp.maximum(jnp.transpose(totals, (1, 2, 3, 4, 0)), 0.0).astype(jnp.bfloat16)


def solution(mesh):
    placed = (
        P(None, "col", "af", None, None),
        P(None, None, None, "af", None),
        P(None, None, None, "af", None),
    )
    return jax.shard_map(
        per_device,
        mesh=mesh,
        in_specs=placed,
        out_specs=P(None, "col", None, None, "af"),
        check_vma=False,
    )
```

```python
import jax
import jax.numpy as jnp
from jax import lax
from jax.sharding import PartitionSpec as P


def extended(block, sides, width):
    for axis, dim in sides:
        count = lax.axis_size(axis)
        forward = [(i, i + 1) for i in range(count - 1)]
        backward = [(target, source) for source, target in forward]
        low = lax.ppermute(
            lax.slice_in_dim(block, block.shape[dim] - width, None, axis=dim), axis, forward
        )
        high = lax.ppermute(lax.slice_in_dim(block, 0, width, axis=dim), axis, backward)
        block = jnp.concatenate([low, block, high], axis=dim)
    return block


def passed_along(array, axis, by):
    peers = lax.axis_size(axis)
    pairs = [(i, i + by) for i in range(peers) if 0 <= i + by < peers]
    return lax.ppermute(array, axis, pairs)


def convolve(volume, kernel, stride, row_pad, out_spec="NDHWC"):
    return lax.conv_general_dilated(
        volume,
        kernel,
        (stride, stride, stride),
        ((0, 0), (row_pad, row_pad), (1, 1)),
        dimension_numbers=("NDHWC", "DHWIO", out_spec),
        preferred_element_type=jnp.float32,
    )


def reduce_scattered(partial):
    chips = lax.axis_size("z")
    mine = lax.axis_index("core")
    blocks = partial.reshape((chips, 2, partial.shape[0] // (2 * chips)) + partial.shape[1:])
    keep = lax.dynamic_index_in_dim(blocks, mine, axis=1, keepdims=False)
    give = lax.dynamic_index_in_dim(blocks, 1 - mine, axis=1, keepdims=False)
    half = keep + lax.ppermute(give, "core", [(0, 1), (1, 0)])
    return lax.all_to_all(half, "z", 0, 0, tiled=True).sum(axis=0)


def per_device(inputs, first_filters, second_filters):
    padded = extended(inputs, (("col", 1),), 1)
    gathered = lax.all_gather(lax.all_gather(padded, "core", axis=2, tiled=True), "z", axis=2, tiled=True)
    own_first = lax.all_to_all(first_filters, ("z", "core"), split_axis=4, concat_axis=3, tiled=True)
    hidden = jnp.maximum(convolve(gathered, own_first, 1, 1), 0.0).astype(jnp.bfloat16)
    lower_plane = passed_along(hidden[:, -1:], "col", 1)
    stacked = jnp.concatenate([lower_plane, hidden], axis=1)
    partial = convolve(stacked, second_filters, 2, 1, out_spec="CNDHW")
    totals = reduce_scattered(partial)
    return jnp.maximum(jnp.transpose(totals, (1, 2, 3, 4, 0)), 0.0).astype(jnp.bfloat16)


def solution(mesh):
    fine = jax.sharding.Mesh(mesh.devices.reshape(mesh.devices.shape[0], -1, 2), ("col", "z", "core"))
    placed = (
        P(None, "col", ("z", "core"), None, None),
        P(None, None, None, ("z", "core"), None),
        P(None, None, None, ("z", "core"), None),
    )
    return jax.shard_map(
        per_device,
        mesh=fine,
        in_specs=placed,
        out_specs=P(None, "col", None, None, ("z", "core")),
        check_vma=False,
    )
```

```python
import jax
import jax.numpy as jnp
from jax import lax
from jax.sharding import PartitionSpec as P


def extended(block, sides, width):
    for axis, dim in sides:
        count = lax.axis_size(axis)
        forward = [(i, i + 1) for i in range(count - 1)]
        backward = [(target, source) for source, target in forward]
        low = lax.ppermute(
            lax.slice_in_dim(block, block.shape[dim] - width, None, axis=dim), axis, forward
        )
        high = lax.ppermute(lax.slice_in_dim(block, 0, width, axis=dim), axis, backward)
        block = jnp.concatenate([low, block, high], axis=dim)
    return block


def passed_along(array, axis, by):
    peers = lax.axis_size(axis)
    pairs = [(i, i + by) for i in range(peers) if 0 <= i + by < peers]
    return lax.ppermute(array, axis, pairs)


def convolve(volume, kernel, stride, row_pad, out_spec="NDHWC"):
    return lax.conv_general_dilated(
        volume,
        kernel,
        (stride, stride, stride),
        ((0, 0), (row_pad, row_pad), (1, 1)),
        dimension_numbers=("NDHWC", "DHWIO", out_spec),
        preferred_element_type=jnp.float32,
    )


def reduce_scattered(partial):
    chips = lax.axis_size("z")
    mine = lax.axis_index("core")
    blocks = partial.reshape((chips, 2, partial.shape[0] // (2 * chips)) + partial.shape[1:])
    keep = lax.dynamic_index_in_dim(blocks, mine, axis=1, keepdims=False)
    give = lax.dynamic_index_in_dim(blocks, 1 - mine, axis=1, keepdims=False)
    half = keep + lax.ppermute(give, "core", [(0, 1), (1, 0)])
    return lax.all_to_all(half, "z", 0, 0, tiled=True).sum(axis=0)


def gathered_rows(block, axis):
    peers = lax.axis_size(axis)
    me = lax.axis_index(axis)
    rows = jnp.transpose(block, (2, 0, 1, 3, 4))[None]
    for bit in reversed(range(peers.bit_length() - 1)):
        pairs = [(i, i ^ (1 << bit)) for i in range(peers)]
        other = lax.ppermute(rows, axis, pairs)
        low = (me // (1 << bit)) % 2 == 0
        rows = jnp.where(low, jnp.stack([rows, other], 1), jnp.stack([other, rows], 1))
        rows = rows.reshape((-1,) + rows.shape[2:])
    rows = rows.reshape((-1,) + rows.shape[2:])
    return jnp.transpose(rows, (1, 2, 0, 3, 4))


def per_device(inputs, first_filters, second_filters):
    padded = extended(inputs, (("col", 1),), 1)
    gathered = gathered_rows(padded, ("z", "core"))
    own_first = lax.all_to_all(first_filters, ("z", "core"), split_axis=4, concat_axis=3, tiled=True)
    hidden = jnp.maximum(convolve(gathered, own_first, 1, 1), 0.0).astype(jnp.bfloat16)
    lower_plane = passed_along(hidden[:, -1:], "col", 1)
    stacked = jnp.concatenate([lower_plane, hidden], axis=1)
    partial = convolve(stacked, second_filters, 2, 1, out_spec="CNDHW")
    totals = reduce_scattered(partial)
    return jnp.maximum(jnp.transpose(totals, (1, 2, 3, 4, 0)), 0.0).astype(jnp.bfloat16)


def solution(mesh):
    fine = jax.sharding.Mesh(mesh.devices.reshape(mesh.devices.shape[0], -1, 2), ("col", "z", "core"))
    placed = (
        P(None, "col", ("z", "core"), None, None),
        P(None, None, None, ("z", "core"), None),
        P(None, None, None, ("z", "core"), None),
    )
    return jax.shard_map(
        per_device,
        mesh=fine,
        in_specs=placed,
        out_specs=P(None, "col", None, None, ("z", "core")),
        check_vma=False,
    )
```

```python
import jax
import jax.numpy as jnp
from jax import lax
from jax.sharding import PartitionSpec as P


def extended(block, sides, width):
    for axis, dim in sides:
        count = lax.axis_size(axis)
        forward = [(i, i + 1) for i in range(count - 1)]
        backward = [(target, source) for source, target in forward]
        low = lax.ppermute(
            lax.slice_in_dim(block, block.shape[dim] - width, None, axis=dim), axis, forward
        )
        high = lax.ppermute(lax.slice_in_dim(block, 0, width, axis=dim), axis, backward)
        block = jnp.concatenate([low, block, high], axis=dim)
    return block


def passed_along(array, axis, by):
    peers = lax.axis_size(axis)
    pairs = [(i, i + by) for i in range(peers) if 0 <= i + by < peers]
    return lax.ppermute(array, axis, pairs)


def convolve(volume, kernel, stride, row_pad, out_spec="NDHWC"):
    return lax.conv_general_dilated(
        volume,
        kernel,
        (stride, stride, stride),
        ((0, 0), (row_pad, row_pad), (1, 1)),
        dimension_numbers=("NDHWC", "DHWIO", out_spec),
        preferred_element_type=jnp.float32,
    )


def reduce_scattered(partial):
    chips = lax.axis_size("z")
    mine = lax.axis_index("core")
    blocks = partial.reshape((chips, 2, partial.shape[0] // (2 * chips)) + partial.shape[1:])
    keep = lax.dynamic_index_in_dim(blocks, mine, axis=1, keepdims=False)
    give = lax.dynamic_index_in_dim(blocks, 1 - mine, axis=1, keepdims=False)
    half = keep + lax.ppermute(give, "core", [(0, 1), (1, 0)])
    return lax.all_to_all(half, "z", 0, 0, tiled=True).sum(axis=0)


def gathered(block, kernel, axis):
    peers = lax.axis_size(axis)
    me = lax.axis_index(axis)
    rows = jnp.transpose(block, (2, 0, 1, 3, 4))[None]
    taps, width, filters = kernel.shape[:3], kernel.shape[3], kernel.shape[4] // peers
    held = kernel.reshape((-1, width, peers, filters)).transpose(2, 0, 1, 3)[None]
    for bit in reversed(range(peers.bit_length() - 1)):
        pairs = [(i, i ^ (1 << bit)) for i in range(peers)]
        mine = (me // (1 << bit)) % 2
        low = mine == 0
        split = held.reshape(held.shape[:1] + (2, -1) + held.shape[2:])
        keep = lax.dynamic_index_in_dim(split, mine, axis=1, keepdims=False)
        give = lax.dynamic_index_in_dim(split, 1 - mine, axis=1, keepdims=False)
        other, got = lax.ppermute((rows, give), axis, pairs)
        rows = jnp.where(low, jnp.stack([rows, other], 1), jnp.stack([other, rows], 1))
        rows = rows.reshape((-1,) + rows.shape[2:])
        held = jnp.where(low, jnp.stack([keep, got], 1), jnp.stack([got, keep], 1))
        held = held.reshape((-1,) + held.shape[2:])
    rows = rows.reshape((-1,) + rows.shape[2:])
    own = held.reshape((peers,) + held.shape[2:]).transpose(1, 0, 2, 3)
    return jnp.transpose(rows, (1, 2, 0, 3, 4)), own.reshape(taps + (peers * width, filters))


def per_device(inputs, first_filters, second_filters):
    padded = extended(inputs, (("col", 1),), 1)
    slab, own_first = gathered(padded, first_filters, ("z", "core"))
    hidden = jnp.maximum(convolve(slab, own_first, 1, 1), 0.0).astype(jnp.bfloat16)
    lower_plane = passed_along(hidden[:, -1:], "col", 1)
    stacked = jnp.concatenate([lower_plane, hidden], axis=1)
    partial = convolve(stacked, second_filters, 2, 1, out_spec="CNDHW")
    totals = reduce_scattered(partial)
    return jnp.maximum(jnp.transpose(totals, (1, 2, 3, 4, 0)), 0.0).astype(jnp.bfloat16)


def solution(mesh):
    fine = jax.sharding.Mesh(mesh.devices.reshape(mesh.devices.shape[0], -1, 2), ("col", "z", "core"))
    placed = (
        P(None, "col", ("z", "core"), None, None),
        P(None, None, None, ("z", "core"), None),
        P(None, None, None, ("z", "core"), None),
    )
    return jax.shard_map(
        per_device,
        mesh=fine,
        in_specs=placed,
        out_specs=P(None, "col", None, None, ("z", "core")),
        check_vma=False,
    )
```

```python
import jax
import jax.numpy as jnp
from jax import lax
from jax.sharding import PartitionSpec as P


def extended(block, sides, width):
    for axis, dim in sides:
        count = lax.axis_size(axis)
        forward = [(i, i + 1) for i in range(count - 1)]
        backward = [(target, source) for source, target in forward]
        low = lax.ppermute(
            lax.slice_in_dim(block, block.shape[dim] - width, None, axis=dim), axis, forward
        )
        high = lax.ppermute(lax.slice_in_dim(block, 0, width, axis=dim), axis, backward)
        block = jnp.concatenate([low, block, high], axis=dim)
    return block


def passed_along(array, axis, by):
    peers = lax.axis_size(axis)
    pairs = [(i, i + by) for i in range(peers) if 0 <= i + by < peers]
    return lax.ppermute(array, axis, pairs)


def convolve(volume, kernel, stride, row_pad, out_spec="NDHWC"):
    return lax.conv_general_dilated(
        volume,
        kernel,
        (stride, stride, stride),
        ((0, 0), (row_pad, row_pad), (1, 1)),
        dimension_numbers=("NDHWC", "DHWIO", out_spec),
        preferred_element_type=jnp.float32,
    )


def reduce_scattered(partial):
    chips = lax.axis_size("z")
    mine = lax.axis_index("core")
    blocks = partial.reshape((chips, 2, partial.shape[0] // (2 * chips)) + partial.shape[1:])
    keep = lax.dynamic_index_in_dim(blocks, mine, axis=1, keepdims=False)
    give = lax.dynamic_index_in_dim(blocks, 1 - mine, axis=1, keepdims=False)
    half = keep + lax.ppermute(give, "core", [(0, 1), (1, 0)])
    return lax.all_to_all(half, "z", 0, 0, tiled=True).sum(axis=0)


def gathered(block, kernel, axis):
    peers = lax.axis_size(axis)
    me = lax.axis_index(axis)
    rows = jnp.transpose(block, (2, 0, 1, 3, 4))[None]
    taps, width, filters = kernel.shape[:3], kernel.shape[3], kernel.shape[4] // peers
    held = kernel.reshape((-1, width, peers, filters)).transpose(2, 0, 1, 3)[None]
    for bit in reversed(range(peers.bit_length() - 1)):
        pairs = [(i, i ^ (1 << bit)) for i in range(peers)]
        mine = (me // (1 << bit)) % 2
        low = mine == 0
        split = held.reshape(held.shape[:1] + (2, -1) + held.shape[2:])
        keep = lax.dynamic_index_in_dim(split, mine, axis=1, keepdims=False)
        give = lax.dynamic_index_in_dim(split, 1 - mine, axis=1, keepdims=False)
        lanes = rows.shape[-1]
        both = jnp.concatenate([rows.reshape(-1, lanes), give.reshape(-1, lanes)])
        both = lax.ppermute(both, axis, pairs)
        other = both[: rows.size // lanes].reshape(rows.shape)
        got = both[rows.size // lanes :].reshape(give.shape)
        rows = jnp.where(low, jnp.stack([rows, other], 1), jnp.stack([other, rows], 1))
        rows = rows.reshape((-1,) + rows.shape[2:])
        held = jnp.where(low, jnp.stack([keep, got], 1), jnp.stack([got, keep], 1))
        held = held.reshape((-1,) + held.shape[2:])
    rows = rows.reshape((-1,) + rows.shape[2:])
    own = held.reshape((peers,) + held.shape[2:]).transpose(1, 0, 2, 3)
    return jnp.transpose(rows, (1, 2, 0, 3, 4)), own.reshape(taps + (peers * width, filters))


def per_device(inputs, first_filters, second_filters):
    padded = extended(inputs, (("col", 1),), 1)
    slab, own_first = gathered(padded, first_filters, ("z", "core"))
    hidden = jnp.maximum(convolve(slab, own_first, 1, 1), 0.0).astype(jnp.bfloat16)
    lower_plane = passed_along(hidden[:, -1:], "col", 1)
    stacked = jnp.concatenate([lower_plane, hidden], axis=1)
    partial = convolve(stacked, second_filters, 2, 1, out_spec="CNDHW")
    totals = reduce_scattered(partial)
    return jnp.maximum(jnp.transpose(totals, (1, 2, 3, 4, 0)), 0.0).astype(jnp.bfloat16)


def solution(mesh):
    fine = jax.sharding.Mesh(mesh.devices.reshape(mesh.devices.shape[0], -1, 2), ("col", "z", "core"))
    placed = (
        P(None, "col", ("z", "core"), None, None),
        P(None, None, None, ("z", "core"), None),
        P(None, None, None, ("z", "core"), None),
    )
    return jax.shard_map(
        per_device,
        mesh=fine,
        in_specs=placed,
        out_specs=P(None, "col", None, None, ("z", "core")),
        check_vma=False,
    )
```

```python
import jax
import jax.numpy as jnp
from jax import lax
from jax.sharding import PartitionSpec as P


def extended(block, sides, width):
    for axis, dim in sides:
        count = lax.axis_size(axis)
        forward = [(i, i + 1) for i in range(count - 1)]
        backward = [(target, source) for source, target in forward]
        low = lax.ppermute(
            lax.slice_in_dim(block, block.shape[dim] - width, None, axis=dim), axis, forward
        )
        high = lax.ppermute(lax.slice_in_dim(block, 0, width, axis=dim), axis, backward)
        block = jnp.concatenate([low, block, high], axis=dim)
    return block


def passed_along(array, axis, by):
    peers = lax.axis_size(axis)
    pairs = [(i, i + by) for i in range(peers) if 0 <= i + by < peers]
    return lax.ppermute(array, axis, pairs)


def convolve(volume, kernel, stride, row_pad, out_spec="NDHWC"):
    return lax.conv_general_dilated(
        volume,
        kernel,
        (stride, stride, stride),
        ((0, 0), (row_pad, row_pad), (1, 1)),
        dimension_numbers=("NDHWC", "DHWIO", out_spec),
        preferred_element_type=jnp.float32,
    )


def reduce_scattered(partial):
    chips = lax.axis_size("z")
    mine = lax.axis_index("core")
    blocks = partial.reshape((chips, 2, partial.shape[0] // (2 * chips)) + partial.shape[1:])
    keep = lax.dynamic_index_in_dim(blocks, mine, axis=1, keepdims=False)
    give = lax.dynamic_index_in_dim(blocks, 1 - mine, axis=1, keepdims=False)
    half = keep + lax.ppermute(give, "core", [(0, 1), (1, 0)])
    return lax.all_to_all(half, "z", 0, 0, tiled=True).sum(axis=0)


def per_device(inputs, first_filters, second_filters):
    own = lax.all_gather(inputs, ("z", "core"), axis=2, tiled=True)
    lower = passed_along(own[:, -1:], "col", 1)
    upper = passed_along(own[:, :1], "col", -1)
    gathered = jnp.concatenate([lower, own, upper], axis=1)
    own_first = lax.all_to_all(first_filters, ("z", "core"), split_axis=4, concat_axis=3, tiled=True)
    hidden = jnp.maximum(convolve(gathered, own_first, 1, 1), 0.0).astype(jnp.bfloat16)
    lower_plane = passed_along(hidden[:, -1:], "col", 1)
    stacked = jnp.concatenate([lower_plane, hidden], axis=1)
    partial = convolve(stacked, second_filters, 2, 1, out_spec="CNDHW")
    totals = reduce_scattered(partial)
    return jnp.maximum(jnp.transpose(totals, (1, 2, 3, 4, 0)), 0.0).astype(jnp.bfloat16)


def solution(mesh):
    fine = jax.sharding.Mesh(mesh.devices.reshape(mesh.devices.shape[0], -1, 2), ("col", "z", "core"))
    placed = (
        P(None, "col", ("z", "core"), None, None),
        P(None, None, None, ("z", "core"), None),
        P(None, None, None, ("z", "core"), None),
    )
    return jax.shard_map(
        per_device,
        mesh=fine,
        in_specs=placed,
        out_specs=P(None, "col", None, None, ("z", "core")),
        check_vma=False,
    )
```

```python
import jax
import jax.numpy as jnp
from jax import lax
from jax.sharding import PartitionSpec as P


def extended(block, sides, width):
    for axis, dim in sides:
        count = lax.axis_size(axis)
        forward = [(i, i + 1) for i in range(count - 1)]
        backward = [(target, source) for source, target in forward]
        low = lax.ppermute(
            lax.slice_in_dim(block, block.shape[dim] - width, None, axis=dim), axis, forward
        )
        high = lax.ppermute(lax.slice_in_dim(block, 0, width, axis=dim), axis, backward)
        block = jnp.concatenate([low, block, high], axis=dim)
    return block


def passed_along(array, axis, by):
    peers = lax.axis_size(axis)
    pairs = [(i, i + by) for i in range(peers) if 0 <= i + by < peers]
    return lax.ppermute(array, axis, pairs)


def convolve(volume, kernel, stride, row_pad, out_spec="NDHWC"):
    return lax.conv_general_dilated(
        volume,
        kernel,
        (stride, stride, stride),
        ((0, 0), (row_pad, row_pad), (1, 1)),
        dimension_numbers=("NDHWC", "DHWIO", out_spec),
        preferred_element_type=jnp.float32,
    )


def convolve_by_taps(volume, kernel):
    samples, depth, rows, cols, width = volume.shape
    taps = kernel.shape[:3]
    filters = kernel.shape[-1]
    flat = jnp.transpose(kernel, (3, 0, 1, 2, 4)).reshape(width, -1)
    products = jnp.dot(volume.reshape(-1, width), flat, preferred_element_type=jnp.float32)
    products = products.reshape((samples, depth, rows, cols, -1))
    products = jnp.pad(products, ((0, 0), (0, 0), (1, 1), (1, 1), (0, 0)))
    out = depth - taps[0] + 1
    total = None
    for a in range(taps[0]):
        for b in range(taps[1]):
            for c in range(taps[2]):
                t = (a * taps[1] + b) * taps[2] + c
                term = products[:, a : a + out, b : b + rows, c : c + cols, t * filters : (t + 1) * filters]
                total = term if total is None else total + term
    return total


def reduce_scattered(partial):
    chips = lax.axis_size("z")
    mine = lax.axis_index("core")
    blocks = partial.reshape((chips, 2, partial.shape[0] // (2 * chips)) + partial.shape[1:])
    keep = lax.dynamic_index_in_dim(blocks, mine, axis=1, keepdims=False)
    give = lax.dynamic_index_in_dim(blocks, 1 - mine, axis=1, keepdims=False)
    half = keep + lax.ppermute(give, "core", [(0, 1), (1, 0)])
    return lax.all_to_all(half, "z", 0, 0, tiled=True).sum(axis=0)


def per_device(inputs, first_filters, second_filters):
    padded = extended(inputs, (("col", 1),), 1)
    gathered = lax.all_gather(lax.all_gather(padded, "core", axis=2, tiled=True), "z", axis=2, tiled=True)
    own_first = lax.all_to_all(first_filters, ("z", "core"), split_axis=4, concat_axis=3, tiled=True)
    hidden = jnp.maximum(convolve_by_taps(gathered, own_first), 0.0).astype(jnp.bfloat16)
    lower_plane = passed_along(hidden[:, -1:], "col", 1)
    stacked = jnp.concatenate([lower_plane, hidden], axis=1)
    partial = convolve(stacked, second_filters, 2, 1, out_spec="CNDHW")
    totals = reduce_scattered(partial)
    return jnp.maximum(jnp.transpose(totals, (1, 2, 3, 4, 0)), 0.0).astype(jnp.bfloat16)


def solution(mesh):
    fine = jax.sharding.Mesh(mesh.devices.reshape(mesh.devices.shape[0], -1, 2), ("col", "z", "core"))
    placed = (
        P(None, "col", ("z", "core"), None, None),
        P(None, None, None, ("z", "core"), None),
        P(None, None, None, ("z", "core"), None),
    )
    return jax.shard_map(
        per_device,
        mesh=fine,
        in_specs=placed,
        out_specs=P(None, "col", None, None, ("z", "core")),
        check_vma=False,
    )
```

```python
import jax
import jax.numpy as jnp
from jax import lax
from jax.sharding import PartitionSpec as P


def extended(block, sides, width):
    for axis, dim in sides:
        count = lax.axis_size(axis)
        forward = [(i, i + 1) for i in range(count - 1)]
        backward = [(target, source) for source, target in forward]
        low = lax.ppermute(
            lax.slice_in_dim(block, block.shape[dim] - width, None, axis=dim), axis, forward
        )
        high = lax.ppermute(lax.slice_in_dim(block, 0, width, axis=dim), axis, backward)
        block = jnp.concatenate([low, block, high], axis=dim)
    return block


def passed_along(array, axis, by):
    peers = lax.axis_size(axis)
    pairs = [(i, i + by) for i in range(peers) if 0 <= i + by < peers]
    return lax.ppermute(array, axis, pairs)


def convolve(volume, kernel, stride, row_pad, out_spec="NDHWC"):
    return lax.conv_general_dilated(
        volume,
        kernel,
        (stride, stride, stride),
        ((0, 0), (row_pad, row_pad), (1, 1)),
        dimension_numbers=("NDHWC", "DHWIO", out_spec),
        preferred_element_type=jnp.float32,
    )


def convolve_by_taps(volume, kernel):
    samples, depth, rows, cols, width = volume.shape
    taps = kernel.shape[:3]
    filters = kernel.shape[-1]
    flat = jnp.transpose(kernel, (3, 0, 1, 2, 4)).reshape(width, -1)
    products = jnp.dot(volume.reshape(-1, width), flat, preferred_element_type=jnp.float32)
    return products.reshape((samples, depth, rows, cols, -1))


def tap_sum(products, kernel, plane, rows, cols):
    products = jnp.pad(products, ((0, 0), (0, 0), (1, 1), (1, 1), (0, 0)))
    taps = kernel.shape[:3]
    filters = kernel.shape[-1]
    out = 1
    total = None
    for a in range(taps[0]):
        for b in range(taps[1]):
            for c in range(taps[2]):
                t = (a * taps[1] + b) * taps[2] + c
                term = products[:, plane + a : plane + a + out, b : b + rows, c : c + cols, t * filters : (t + 1) * filters]
                total = term if total is None else total + term
    return total


def reduce_scattered(partial):
    chips = lax.axis_size("z")
    mine = lax.axis_index("core")
    blocks = partial.reshape((chips, 2, partial.shape[0] // (2 * chips)) + partial.shape[1:])
    keep = lax.dynamic_index_in_dim(blocks, mine, axis=1, keepdims=False)
    give = lax.dynamic_index_in_dim(blocks, 1 - mine, axis=1, keepdims=False)
    half = keep + lax.ppermute(give, "core", [(0, 1), (1, 0)])
    return lax.all_to_all(half, "z", 0, 0, tiled=True).sum(axis=0)


def per_device(inputs, first_filters, second_filters):
    padded = extended(inputs, (("col", 1),), 1)
    gathered = lax.all_gather(lax.all_gather(padded, "core", axis=2, tiled=True), "z", axis=2, tiled=True)
    own_first = lax.all_to_all(first_filters, ("z", "core"), split_axis=4, concat_axis=3, tiled=True)
    products = convolve_by_taps(gathered, own_first)
    rows, cols = gathered.shape[2], gathered.shape[3]
    last = jnp.maximum(tap_sum(products, own_first, 1, rows, cols), 0.0).astype(jnp.bfloat16)
    lower_plane = passed_along(last, "col", 1)
    products, _ = lax.optimization_barrier((products, last))
    first = jnp.maximum(tap_sum(products, own_first, 0, rows, cols), 0.0).astype(jnp.bfloat16)
    stacked = jnp.concatenate([lower_plane, first, last], axis=1)
    partial = convolve(stacked, second_filters, 2, 1, out_spec="CNDHW")
    totals = reduce_scattered(partial)
    return jnp.maximum(jnp.transpose(totals, (1, 2, 3, 4, 0)), 0.0).astype(jnp.bfloat16)


def solution(mesh):
    fine = jax.sharding.Mesh(mesh.devices.reshape(mesh.devices.shape[0], -1, 2), ("col", "z", "core"))
    placed = (
        P(None, "col", ("z", "core"), None, None),
        P(None, None, None, ("z", "core"), None),
        P(None, None, None, ("z", "core"), None),
    )
    return jax.shard_map(
        per_device,
        mesh=fine,
        in_specs=placed,
        out_specs=P(None, "col", None, None, ("z", "core")),
        check_vma=False,
    )
```

```python
import jax
import jax.numpy as jnp
from jax import lax
from jax.sharding import PartitionSpec as P


def extended(block, sides, width):
    for axis, dim in sides:
        count = lax.axis_size(axis)
        forward = [(i, i + 1) for i in range(count - 1)]
        backward = [(target, source) for source, target in forward]
        low = lax.ppermute(
            lax.slice_in_dim(block, block.shape[dim] - width, None, axis=dim), axis, forward
        )
        high = lax.ppermute(lax.slice_in_dim(block, 0, width, axis=dim), axis, backward)
        block = jnp.concatenate([low, block, high], axis=dim)
    return block


def passed_along(array, axis, by):
    peers = lax.axis_size(axis)
    pairs = [(i, i + by) for i in range(peers) if 0 <= i + by < peers]
    return lax.ppermute(array, axis, pairs)


def convolve(volume, kernel, stride, row_pad, out_spec="NDHWC"):
    return lax.conv_general_dilated(
        volume,
        kernel,
        (stride, stride, stride),
        ((0, 0), (row_pad, row_pad), (1, 1)),
        dimension_numbers=("NDHWC", "DHWIO", out_spec),
        preferred_element_type=jnp.float32,
    )


def convolve_by_taps(volume, kernel):
    samples, depth, rows, cols, width = volume.shape
    taps = kernel.shape[:3]
    filters = kernel.shape[-1]
    flat = jnp.transpose(kernel, (3, 0, 1, 2, 4)).reshape(width, -1)
    products = jnp.dot(volume.reshape(-1, width), flat, preferred_element_type=jnp.float32)
    return products.reshape((samples, depth, rows, cols, -1))


def tap_sum(products, kernel, plane, rows, cols):
    products = jnp.pad(products, ((0, 0), (0, 0), (1, 1), (1, 1), (0, 0)))
    taps = kernel.shape[:3]
    filters = kernel.shape[-1]
    out = 1
    total = None
    for a in range(taps[0]):
        for b in range(taps[1]):
            for c in range(taps[2]):
                t = (a * taps[1] + b) * taps[2] + c
                term = products[:, plane + a : plane + a + out, b : b + rows, c : c + cols, t * filters : (t + 1) * filters]
                total = term if total is None else total + term
    return total


def reduce_scattered(partial):
    chips = lax.axis_size("z")
    mine = lax.axis_index("core")
    blocks = partial.reshape((chips, 2, partial.shape[0] // (2 * chips)) + partial.shape[1:])
    keep = lax.dynamic_index_in_dim(blocks, mine, axis=1, keepdims=False)
    give = lax.dynamic_index_in_dim(blocks, 1 - mine, axis=1, keepdims=False)
    half = keep + lax.ppermute(give, "core", [(0, 1), (1, 0)])
    return lax.all_to_all(half, "z", 0, 0, tiled=True).sum(axis=0)


def per_device(inputs, first_filters, second_filters):
    padded = extended(inputs, (("col", 1),), 1)
    gathered = lax.all_gather(lax.all_gather(padded, "core", axis=2, tiled=True), "z", axis=2, tiled=True)
    own_first = lax.all_to_all(first_filters, ("z", "core"), split_axis=4, concat_axis=3, tiled=True)
    products = convolve_by_taps(gathered, own_first)
    rows, cols = gathered.shape[2], gathered.shape[3]
    last = jnp.maximum(tap_sum(products, own_first, 1, rows, cols), 0.0).astype(jnp.bfloat16)
    lower_plane = passed_along(last, "col", 1)
    products, _ = lax.optimization_barrier((products, last))
    first = jnp.maximum(tap_sum(products, own_first, 0, rows, cols), 0.0).astype(jnp.bfloat16)
    own = jnp.concatenate([first, last], axis=1)
    partial = convolve(own, second_filters[1:], 2, 1, out_spec="CNDHW")
    partial = partial + convolve(lower_plane, second_filters[:1], 2, 1, out_spec="CNDHW")
    totals = reduce_scattered(partial)
    return jnp.maximum(jnp.transpose(totals, (1, 2, 3, 4, 0)), 0.0).astype(jnp.bfloat16)


def solution(mesh):
    fine = jax.sharding.Mesh(mesh.devices.reshape(mesh.devices.shape[0], -1, 2), ("col", "z", "core"))
    placed = (
        P(None, "col", ("z", "core"), None, None),
        P(None, None, None, ("z", "core"), None),
        P(None, None, None, ("z", "core"), None),
    )
    return jax.shard_map(
        per_device,
        mesh=fine,
        in_specs=placed,
        out_specs=P(None, "col", None, None, ("z", "core")),
        check_vma=False,
    )
```

```python
import jax
import jax.numpy as jnp
from jax import lax
from jax.sharding import PartitionSpec as P


def extended(block, sides, width):
    for axis, dim in sides:
        count = lax.axis_size(axis)
        forward = [(i, i + 1) for i in range(count - 1)]
        backward = [(target, source) for source, target in forward]
        low = lax.ppermute(
            lax.slice_in_dim(block, block.shape[dim] - width, None, axis=dim), axis, forward
        )
        high = lax.ppermute(lax.slice_in_dim(block, 0, width, axis=dim), axis, backward)
        block = jnp.concatenate([low, block, high], axis=dim)
    return block


def passed_along(array, axis, by):
    peers = lax.axis_size(axis)
    pairs = [(i, i + by) for i in range(peers) if 0 <= i + by < peers]
    return lax.ppermute(array, axis, pairs)


def convolve(volume, kernel, stride, row_pad, out_spec="NDHWC"):
    return lax.conv_general_dilated(
        volume,
        kernel,
        (stride, stride, stride),
        ((0, 0), (row_pad, row_pad), (1, 1)),
        dimension_numbers=("NDHWC", "DHWIO", out_spec),
        preferred_element_type=jnp.float32,
    )


def convolve_by_taps(volume, kernel):
    samples, depth, rows, cols, width = volume.shape
    taps = kernel.shape[:3]
    filters = kernel.shape[-1]
    flat = jnp.transpose(kernel, (3, 0, 1, 2, 4)).reshape(width, -1)
    products = jnp.dot(volume.reshape(-1, width), flat, preferred_element_type=jnp.float32)
    return products.reshape((samples, depth, rows, cols, -1))


def tap_sum(products, kernel, plane, rows, cols):
    products = jnp.pad(products, ((0, 0), (0, 0), (1, 1), (1, 1), (0, 0)))
    taps = kernel.shape[:3]
    filters = kernel.shape[-1]
    out = 1
    total = None
    for a in range(taps[0]):
        for b in range(taps[1]):
            for c in range(taps[2]):
                t = (a * taps[1] + b) * taps[2] + c
                term = products[:, plane + a : plane + a + out, b : b + rows, c : c + cols, t * filters : (t + 1) * filters]
                total = term if total is None else total + term
    return total


def reduce_scattered(partial):
    peers = lax.axis_size(("z", "core"))
    blocks = partial.reshape((peers, partial.shape[0] // peers) + partial.shape[1:])
    return lax.all_to_all(blocks, ("z", "core"), 0, 0, tiled=True).sum(axis=0)


def per_device(inputs, first_filters, second_filters):
    padded = extended(inputs, (("col", 1),), 1)
    gathered = lax.all_gather(lax.all_gather(padded, "core", axis=2, tiled=True), "z", axis=2, tiled=True)
    own_first = lax.all_to_all(first_filters, ("z", "core"), split_axis=4, concat_axis=3, tiled=True)
    products = convolve_by_taps(gathered, own_first)
    rows, cols = gathered.shape[2], gathered.shape[3]
    last = jnp.maximum(tap_sum(products, own_first, 1, rows, cols), 0.0).astype(jnp.bfloat16)
    lower_plane = passed_along(last, "col", 1)
    products, _ = lax.optimization_barrier((products, last))
    first = jnp.maximum(tap_sum(products, own_first, 0, rows, cols), 0.0).astype(jnp.bfloat16)
    own = jnp.concatenate([first, last], axis=1)
    partial = convolve(own, second_filters[1:], 2, 1, out_spec="CNDHW")
    partial = partial + convolve(lower_plane, second_filters[:1], 2, 1, out_spec="CNDHW")
    totals = reduce_scattered(partial)
    return jnp.maximum(jnp.transpose(totals, (1, 2, 3, 4, 0)), 0.0).astype(jnp.bfloat16)


def solution(mesh):
    fine = jax.sharding.Mesh(mesh.devices.reshape(mesh.devices.shape[0], -1, 2), ("col", "z", "core"))
    placed = (
        P(None, "col", ("z", "core"), None, None),
        P(None, None, None, ("z", "core"), None),
        P(None, None, None, ("z", "core"), None),
    )
    return jax.shard_map(
        per_device,
        mesh=fine,
        in_specs=placed,
        out_specs=P(None, "col", None, None, ("z", "core")),
        check_vma=False,
    )
```

```python
import jax
import jax.numpy as jnp
from jax import lax
from jax.sharding import PartitionSpec as P


def extended(block, sides, width):
    for axis, dim in sides:
        count = lax.axis_size(axis)
        forward = [(i, i + 1) for i in range(count - 1)]
        backward = [(target, source) for source, target in forward]
        low = lax.ppermute(
            lax.slice_in_dim(block, block.shape[dim] - width, None, axis=dim), axis, forward
        )
        high = lax.ppermute(lax.slice_in_dim(block, 0, width, axis=dim), axis, backward)
        block = jnp.concatenate([low, block, high], axis=dim)
    return block


def passed_along(array, axis, by):
    peers = lax.axis_size(axis)
    pairs = [(i, i + by) for i in range(peers) if 0 <= i + by < peers]
    return lax.ppermute(array, axis, pairs)


def convolve(volume, kernel, stride, row_pad, out_spec="NDHWC"):
    return lax.conv_general_dilated(
        volume,
        kernel,
        (stride, stride, stride),
        ((0, 0), (row_pad, row_pad), (1, 1)),
        dimension_numbers=("NDHWC", "DHWIO", out_spec),
        preferred_element_type=jnp.float32,
    )


def convolve_by_taps(volume, kernel):
    samples, depth, rows, cols, width = volume.shape
    taps = kernel.shape[:3]
    filters = kernel.shape[-1]
    flat = jnp.transpose(kernel, (3, 0, 1, 2, 4)).reshape(width, -1)
    products = jnp.dot(volume.reshape(-1, width), flat, preferred_element_type=jnp.float32)
    return products.reshape((samples, depth, rows, cols, -1))


def tap_sum(products, kernel, plane, rows, cols):
    products = jnp.pad(products, ((0, 0), (0, 0), (1, 1), (1, 1), (0, 0)))
    taps = kernel.shape[:3]
    filters = kernel.shape[-1]
    out = 1
    total = None
    for a in range(taps[0]):
        for b in range(taps[1]):
            for c in range(taps[2]):
                t = (a * taps[1] + b) * taps[2] + c
                term = products[:, plane + a : plane + a + out, b : b + rows, c : c + cols, t * filters : (t + 1) * filters]
                total = term if total is None else total + term
    return total


def reduce_scattered(partial):
    chips = lax.axis_size("z")
    mine = lax.axis_index("core")
    blocks = partial.reshape((chips, 2, partial.shape[0] // (2 * chips)) + partial.shape[1:])
    keep = lax.dynamic_index_in_dim(blocks, mine, axis=1, keepdims=False)
    give = lax.dynamic_index_in_dim(blocks, 1 - mine, axis=1, keepdims=False)
    half = keep + lax.ppermute(give, "core", [(0, 1), (1, 0)])
    return lax.all_to_all(half, "z", 0, 0, tiled=True).sum(axis=0)


def per_device(inputs, first_filters, second_filters):
    padded = extended(inputs, (("col", 1),), 1)
    gathered = lax.all_gather(padded, ("z", "core"), axis=2, tiled=True)
    own_first = lax.all_to_all(first_filters, ("z", "core"), split_axis=4, concat_axis=3, tiled=True)
    products = convolve_by_taps(gathered, own_first)
    rows, cols = gathered.shape[2], gathered.shape[3]
    last = jnp.maximum(tap_sum(products, own_first, 1, rows, cols), 0.0).astype(jnp.bfloat16)
    lower_plane = passed_along(last, "col", 1)
    products, _ = lax.optimization_barrier((products, last))
    first = jnp.maximum(tap_sum(products, own_first, 0, rows, cols), 0.0).astype(jnp.bfloat16)
    own = jnp.concatenate([first, last], axis=1)
    partial = convolve(own, second_filters[1:], 2, 1, out_spec="CNDHW")
    partial = partial + convolve(lower_plane, second_filters[:1], 2, 1, out_spec="CNDHW")
    totals = reduce_scattered(partial)
    return jnp.maximum(jnp.transpose(totals, (1, 2, 3, 4, 0)), 0.0).astype(jnp.bfloat16)


def solution(mesh):
    fine = jax.sharding.Mesh(mesh.devices.reshape(mesh.devices.shape[0], -1, 2), ("col", "z", "core"))
    placed = (
        P(None, "col", ("z", "core"), None, None),
        P(None, None, None, ("z", "core"), None),
        P(None, None, None, ("z", "core"), None),
    )
    return jax.shard_map(
        per_device,
        mesh=fine,
        in_specs=placed,
        out_specs=P(None, "col", None, None, ("z", "core")),
        check_vma=False,
    )
```
